256 devices in a mesh: pp: 8 (over x, core), ep: 32 (over z, y).
Axes of the slice: x: 4, y: 4, z: 8, core: 2. Of those that a mesh axis runs over, the one named last changes fastest.
Arguments:
- tokens: bfloat16 [512, 2048], P('ep'), may hold values from -6 to 6
- routes: int32 [8, 512, 8], P('pp'), may hold values from 0 to 31, all different within a row; in each aligned block of 16 rows (0 to 15, 16 to 31, ..., all dimensions but the last counted through in order) at most 5 rows name the same one
- combine: float32 [8, 512, 8], P('pp', 'ep'), may hold values from 0.05 to 0.5
- norm_gain: float32 [8, 2048], P('pp'), may hold values from 0.5 to 1.5
- expert_in: bfloat16 [8, 32, 2048, 1536], P('pp', 'ep'), may hold values from -0.125 to 0.125
- expert_out: bfloat16 [8, 32, 768, 2048], P('pp', 'ep'), may hold values from -0.21875 to 0.21875
Outputs:
- section_out: bfloat16 [8, 512, 2048], P('pp', 'ep')
The draws below stay inside these ranges and needn't reach their ends.
Inputs may be any that keep to these rules, and one draw needn't show every extreme that they name: `routes`: each row names 8 different experts. Within the 16 rows of one device (rows i * 16 to (i + 1) * 16 - 1 of one layer) no expert is named more than 5 times, and some such block names some expert exactly 5 times.
All inputs are finite; a program needn't handle non-finite values.
Results may differ from the reference program's by a relative error of at most 0.028.
Values may be sent and summed in bfloat16 or wider, within the bound.
No kernel may reach another device: no remote copies, remote signals or barrier semaphores. Data moves between devices by JAX's collectives and lax.ppermute only.
A program may use at most 64 MiB of HBM per device.

```python
import math
import jax
import jax.numpy as jnp
import numpy as np
from jax import lax

D = 2048
H = 768
TOK_DEV = 16
EXPERTS = 32
TOP = 8
CAP = 5
TOKENS = 512
N_PP = 8
N_EP = 32


def shard_levels(own_key, dims, split, smallest, largest):
    factor_of, own = 1.0, jax.random.fold_in(own_key, 6)
    for position, blocks in split:
        heights = jnp.exp(jax.random.uniform(jax.random.fold_in(own, position), (blocks,), jnp.float32, smallest / len(split), largest / len(split)))
        factor_of = factor_of * jnp.repeat(heights, dims[position] // blocks).reshape([-1 if axis == position else 1 for axis in range(len(dims))])
    return factor_of


def assign_block(stream_key, own, number, rows, count, top, limit, skew):
    sequence = jax.random.permutation(stream_key, count)
    heavy_load, ordinary = shares(count, rows * top, limit, skew, True), shares(count, rows * top, limit, skew, False)
    places = jnp.arange(count)

    def named(tallies, rotation):
        used = int((tallies > 0).sum())
        fixed = max(1, used // 4)
        shifted = fixed + (places - fixed + rotation * (used - fixed)) % max(1, count - fixed)
        return jnp.zeros((count,), jnp.int32).at[sequence[jnp.where(places < fixed, places, shifted)]].set(jnp.asarray(tallies, jnp.int32))

    tallies = jnp.where(number % 4 == 0, named(heavy_load, number // 4), named(ordinary, number - number // 4 - 1))
    mixed = jax.random.permutation(jax.random.fold_in(own, 3), count)
    giver, receiver = mixed[0:count // 2 * 2:2], mixed[1:count // 2 * 2:2]
    slack = jnp.minimum(tallies[giver] - 1, limit - tallies[receiver]) // 2
    slack = jnp.where((giver == sequence[0]) | (receiver == sequence[0]) | (tallies[receiver] == 0), 0, jnp.maximum(slack, 0))
    shifted = jax.random.randint(jax.random.fold_in(own, 4), (count // 2,), 0, 1 << 20) % (slack + 1)
    tallies = tallies.at[giver].add(-shifted).at[receiver].add(shifted)
    members = jnp.searchsorted(jnp.cumsum(tallies), jnp.arange(rows * top), side="right").astype(jnp.int32)
    table = members.reshape(top, rows).T
    table = table[jax.random.permutation(jax.random.fold_in(own, 1), rows)]
    rotation = jax.random.randint(jax.random.fold_in(own, 2), (rows, 1), 0, top)
    return jnp.take_along_axis(table, (jnp.arange(top)[None, :] + rotation) % top, axis=1)


def shares(count, total, reach, slope, full):
    weights = [(1 << 20) // math.isqrt(rank ** slope) + 1 for rank in range(1, count + 1)]
    largest = reach if full else min(reach, max(-(-total // count), total * weights[0] // sum(weights)))
    least = 1 if total - largest >= count - 1 else 0
    counts, spare = [largest] + [least] * (count - 1), total - largest - least * (count - 1)
    while spare > 0:
        movable = [i for i in range(1, count) if counts[i] < largest] or [i for i in range(1, count) if counts[i] < reach]
        whole, remaining = sum([weights[i] for i in movable]), spare
        for i in movable:
            more = min(reach - counts[i], max(1, remaining * weights[i] // whole), spare)
            counts[i] = counts[i] + more
            spare = spare - more
    return np.array(counts)


def centred(stream_key, extent, deviation, most, cuts=(), held_as=jnp.bfloat16):
    loudness = shard_levels(stream_key, extent, cuts, -0.22, 0.18) if cuts else 1.0
    result = jax.random.normal(stream_key, extent, jnp.float32) * deviation * loudness
    return jnp.minimum(jnp.maximum(result, -most), most).astype(held_as)


def setup_inputs(seed: int = 0) -> dict:
    splits = jax.random.split(jax.random.key(seed), 7)
    tokens = centred(splits[0], (TOKENS, D), 1.0, 6.0, ((0, 32),))
    routes_keys = jax.random.split(jax.random.fold_in(splits[1], 1), N_PP * TOKENS // TOK_DEV)
    routes_turns = jax.random.permutation(jax.random.fold_in(splits[1], 3), N_PP * TOKENS // TOK_DEV)
    routes = jax.vmap(lambda own, number: assign_block(jax.random.fold_in(splits[1], 2), own, number, TOK_DEV, EXPERTS, TOP, CAP, 2))(routes_keys, routes_turns).reshape((N_PP, TOKENS, TOP))
    combine = jnp.clip(jnp.exp(math.log(0.5) - 2.3025851 * jax.random.uniform(splits[2], (N_PP, TOKENS, TOP), jnp.float32) ** shard_levels(splits[2], (N_PP, TOKENS, TOP), ((0, 8), (1, 32)), -0.2, 0.2)), 0.05, 0.5)
    norm_gain = jnp.clip(1.0 + 0.1 * jax.random.normal(splits[3], (N_PP, D), jnp.float32), 0.5, 1.5)
    expert_in = centred(splits[4], (N_PP, EXPERTS, D, 2 * H), D ** -0.5, 0.125, ((0, 8), (1, 32)))
    expert_out = centred(splits[5], (N_PP, EXPERTS, H, D), H ** -0.5, 0.21875, ((0, 8), (1, 32)))
    return {"tokens": tokens, "routes": routes, "combine": combine, "norm_gain": norm_gain, "expert_in": expert_in, "expert_out": expert_out}


def reference(tokens, routes, combine, norm_gain, expert_in, expert_out):
    current = tokens
    layers_out = []
    for section_index in range(N_PP):
        widened = current.astype(jnp.float32)
        scale = lax.rsqrt(lax.optimization_barrier(jnp.mean(widened * widened, axis=-1, keepdims=True)) + 1e-06)
        normed = (widened * scale * norm_gain[section_index][None, :]).astype(jnp.bfloat16)
        route_rows = routes[section_index]
        weight_rows = combine[section_index]

        def one_expert(totals, packed):
            expert_id, first_weights, second_weights = packed
            chosen = route_rows == expert_id
            per_token = lax.optimization_barrier(jnp.sum(jnp.where(chosen, weight_rows, 0.0), axis=1))
            routed = jnp.any(chosen, axis=1)
            positions = jnp.nonzero(routed, size=N_EP * CAP, fill_value=0)[0].astype(jnp.int32)
            usable = jnp.arange(N_EP * CAP, dtype=jnp.int32) < jnp.sum(routed.astype(jnp.int32))
            gathered = normed[positions]
            projected = jnp.dot(gathered, first_weights, preferred_element_type=jnp.float32)
            hidden = (jax.nn.silu(projected[:, :H]) * projected[:, H:]).astype(jnp.bfloat16)
            expert_rows = jnp.dot(hidden, second_weights, preferred_element_type=jnp.float32).astype(jnp.bfloat16)
            expert_rows = lax.optimization_barrier(expert_rows).astype(jnp.float32)
            weighted = jnp.where(usable, per_token[positions], 0.0)[:, None] * expert_rows
            return (totals.at[positions].add(weighted), None)
        totals, _ = lax.scan(one_expert, jnp.zeros((TOKENS, D), jnp.float32), (jnp.arange(EXPERTS, dtype=jnp.int32), expert_in[section_index], expert_out[section_index]))
        current = (widened + totals).astype(jnp.bfloat16)
        layers_out.append(current)
    return jnp.stack(layers_out)
```

```python
import jax
import jax.numpy as jnp
from jax import lax
from jax.sharding import PartitionSpec as P


def shards(tokens, routes, combine, norm_gain, expert_in, expert_out):
    group_size = lax.axis_size("ep")
    sections = lax.axis_size("pp")
    section_id = lax.axis_index("pp")
    member = lax.axis_index("ep")
    tok_dev, model_width = tokens.shape
    top_count = routes.shape[2]
    capacity = tok_dev * top_count * 5 // (4 * group_size)
    hidden_units = expert_out.shape[2]
    slot_count = group_size * capacity
    token_count = routes.shape[1]

    section_routes = routes[0]
    mine = section_routes == member
    hit = jnp.any(mine, axis=1)
    all_combine = lax.all_gather(combine[0], "ep", axis=0, tiled=True)
    token_weight = jnp.sum(jnp.where(mine, all_combine, 0.0), axis=1)
    hit_blocks = hit.astype(jnp.int32).reshape(group_size, tok_dev)
    rank = jnp.cumsum(hit_blocks, axis=1) - hit_blocks
    slot_of = (jnp.arange(group_size, dtype=jnp.int32)[:, None] * capacity + rank).reshape(token_count)
    picker = (hit[None, :] & (slot_of[None, :] == jnp.arange(slot_count, dtype=jnp.int32)[:, None])).astype(
        jnp.bfloat16
    )
    first_weights = expert_in[0, 0]
    second_weights = expert_out[0, 0]
    gain_row = norm_gain[0]

    def layer(current):
        widened = current.astype(jnp.float32)
        scale = lax.rsqrt(jnp.mean(widened * widened, axis=-1, keepdims=True) + 1e-06)
        normed = (widened * scale * gain_row[None, :]).astype(jnp.bfloat16)
        gathered = lax.all_gather(normed, "ep", axis=0, tiled=True)
        rows = jnp.dot(picker, gathered, preferred_element_type=jnp.float32).astype(jnp.bfloat16)
        projected = jnp.dot(rows, first_weights, preferred_element_type=jnp.float32)
        hidden = (jax.nn.silu(projected[:, :hidden_units]) * projected[:, hidden_units:]).astype(jnp.bfloat16)
        produced = jnp.dot(hidden, second_weights, preferred_element_type=jnp.float32).astype(jnp.bfloat16)
        scattered = jnp.dot(picker.T, produced, preferred_element_type=jnp.float32)
        weighted = scattered * token_weight[:, None]
        blended = lax.psum_scatter(weighted, "ep", scatter_dimension=0, tiled=True)
        return (widened + blended).astype(jnp.bfloat16)

    current = tokens
    for turn_index in range(sections):
        current = jnp.where(section_id == turn_index, layer(current), current)
        if turn_index + 1 < sections:
            arriving = lax.ppermute(current, "pp", [(turn_index, turn_index + 1)])
            current = jnp.where(section_id == turn_index + 1, arriving, current)
    return current[None]


def solution(mesh):
    placed = (
        P("ep", None),
        P("pp", None, None),
        P("pp", "ep", None),
        P("pp", None),
        P("pp", "ep", None, None),
        P("pp", "ep", None, None),
    )
    return jax.shard_map(
        shards, mesh=mesh, in_specs=placed, out_specs=P("pp", "ep", None), check_vma=False
    )
```

```python
import jax
import jax.numpy as jnp
from jax import lax
from jax.sharding import PartitionSpec as P


def shards(tokens, routes, combine, norm_gain, expert_in, expert_out):
    group_size = lax.axis_size("ep")
    sections = lax.axis_size("pp")
    section_id = lax.axis_index("pp")
    member = lax.axis_index("ep")
    tok_dev, model_width = tokens.shape
    top_count = routes.shape[2]
    capacity = tok_dev * top_count * 5 // (4 * group_size)
    hidden_units = expert_out.shape[2]
    slot_count = group_size * capacity
    section_routes = routes[0]
    start_row = member * tok_dev
    own_routes = lax.dynamic_slice_in_dim(section_routes, start_row, tok_dev, 0)
    flat_routes = (own_routes.reshape(-1) - member) % group_size
    experts_axis = jnp.arange(group_size, dtype=jnp.int32)
    one_hot = (flat_routes[:, None] == experts_axis[None, :]).astype(jnp.int32)
    earlier = jnp.cumsum(one_hot, axis=0) - one_hot
    rank_of = jnp.sum(earlier * one_hot, axis=1)
    slot_of = flat_routes * capacity + rank_of
    slot_grid = slot_of[None, :] == jnp.arange(slot_count, dtype=jnp.int32)[:, None]
    slot_grid = slot_grid.reshape(slot_count, tok_dev, top_count)
    picker = jnp.any(slot_grid, axis=2).astype(jnp.bfloat16)
    weigher = jnp.sum(jnp.where(slot_grid, combine[0][None, :, :], 0.0), axis=2).T
    first_weights = expert_in[0, 0]
    second_weights = expert_out[0, 0]
    gain_row = norm_gain[0]

    def exchange(blocks, turn_index, sign):
        base = turn_index * group_size
        moved = [blocks[0]]
        for k in range(1, group_size):
            pairs = [(base + i, base + (i + sign * k) % group_size) for i in range(group_size)]
            moved.append(lax.ppermute(blocks[k], ("pp", "ep"), pairs))
        return jnp.stack(moved)

    current = tokens
    result = tokens
    for turn_index in range(sections):
        widened = current.astype(jnp.float32)
        scale = lax.rsqrt(jnp.mean(widened * widened, axis=-1, keepdims=True) + 1e-06)
        normed = (widened * scale * gain_row[None, :]).astype(jnp.bfloat16)
        packed = jnp.dot(picker, normed, preferred_element_type=jnp.float32).astype(jnp.bfloat16)
        packed = packed.reshape(group_size, capacity, model_width)
        arrived = exchange(packed, turn_index, 1)
        rows_flat = arrived.reshape(slot_count, model_width)
        projected = jnp.dot(rows_flat, first_weights, preferred_element_type=jnp.float32)
        hidden = (jax.nn.silu(projected[:, :hidden_units]) * projected[:, hidden_units:]).astype(
            jnp.bfloat16
        )
        produced_rows = jnp.dot(hidden, second_weights, preferred_element_type=jnp.float32).astype(
            jnp.bfloat16
        )
        produced = produced_rows.reshape(arrived.shape)
        returned = exchange(produced, turn_index, -1)
        blended = jnp.dot(
            weigher,
            returned.reshape(slot_count, model_width).astype(jnp.float32),
            precision=lax.Precision.HIGHEST,
        )
        output = (widened + blended).astype(jnp.bfloat16)
        result = jnp.where(section_id == turn_index, output, result)
        if turn_index + 1 < sections:
            arriving = lax.ppermute(output, "pp", [(turn_index, turn_index + 1)])
            current = jnp.where(section_id == turn_index + 1, arriving, current)
    return result[None]


def solution(mesh):
    placed = (
        P("ep", None),
        P("pp", None, None),
        P("pp", "ep", None),
        P("pp", None),
        P("pp", "ep", None, None),
        P("pp", "ep", None, None),
    )
    return jax.shard_map(
        shards, mesh=mesh, in_specs=placed, out_specs=P("pp", "ep", None), check_vma=False
    )
```

```python
import jax
import jax.numpy as jnp
from jax import lax
from jax.sharding import Mesh
from jax.sharding import PartitionSpec as P


def from_behind(array, axis, by):
    count = lax.axis_size(axis)
    pairs = [(i, i + by) for i in range(count) if 0 <= i + by < count]
    return lax.ppermute(array, axis, pairs)


def shards(tokens, routes, combine, norm_gain, expert_in, expert_out):
    outer = lax.axis_size("ez")
    inner = lax.axis_size("ey")
    group_size = outer * inner
    sections = lax.axis_size("pp")
    section_id = lax.axis_index("pp")
    member = lax.axis_index("ez") * inner + lax.axis_index("ey")
    tok_dev, model_width = tokens.shape
    top_count = routes.shape[2]
    capacity = tok_dev * top_count * 5 // (4 * group_size)
    hidden_units = expert_out.shape[2]
    slot_count = group_size * capacity
    section_routes = routes[0]
    experts_axis = jnp.arange(group_size, dtype=jnp.int32)
    start_row = member * tok_dev
    own_routes = lax.dynamic_slice_in_dim(section_routes, start_row, tok_dev, 0)
    flat_routes = own_routes.reshape(-1)
    one_hot = (flat_routes[:, None] == experts_axis[None, :]).astype(jnp.int32)
    earlier = jnp.cumsum(one_hot, axis=0) - one_hot
    rank_of = jnp.sum(earlier * one_hot, axis=1)
    slot_of = flat_routes * capacity + rank_of
    slot_grid = slot_of[None, :] == jnp.arange(slot_count, dtype=jnp.int32)[:, None]
    slot_grid = slot_grid.reshape(slot_count, tok_dev, top_count)
    picker = jnp.any(slot_grid, axis=2).astype(jnp.bfloat16).reshape(outer, inner, capacity, tok_dev)
    weigher = jnp.sum(jnp.where(slot_grid, combine[0][None, :, :], 0.0), axis=2).T
    weigher = weigher.reshape(tok_dev, outer, inner, capacity)
    first_weights = expert_in[0, 0]
    second_weights = expert_out[0, 0]
    gain_row = norm_gain[0]
    current = tokens
    result = tokens
    for turn_index in range(sections):
        widened = current.astype(jnp.float32)
        scale = lax.rsqrt(jnp.mean(widened * widened, axis=-1, keepdims=True) + 1e-06)
        normed = (widened * scale * gain_row[None, :]).astype(jnp.bfloat16)
        packed = jnp.einsum("abct,td->abcd", picker, normed, preferred_element_type=jnp.float32)
        packed = packed.astype(jnp.bfloat16)
        stage = lax.all_to_all(packed, "ey", 1, 1, tiled=True)
        arrived = lax.all_to_all(stage, "ez", 0, 0, tiled=True)
        projected = jnp.einsum("abcd,dh->abch", arrived, first_weights, preferred_element_type=jnp.float32)
        hidden = (jax.nn.silu(projected[..., :hidden_units]) * projected[..., hidden_units:]).astype(
            jnp.bfloat16
        )
        produced = jnp.einsum("abch,hd->abcd", hidden, second_weights, preferred_element_type=jnp.float32)
        produced = produced.astype(jnp.bfloat16)
        stage = lax.all_to_all(produced, "ez", 0, 0, tiled=True)
        returned = lax.all_to_all(stage, "ey", 1, 1, tiled=True)
        blended = jnp.einsum(
            "tabc,abcd->td",
            weigher,
            returned.astype(jnp.float32),
            precision=lax.Precision.HIGHEST,
        )
        output = (widened + blended).astype(jnp.bfloat16)
        result = jnp.where(section_id == turn_index, output, result)
        if turn_index + 1 < sections:
            arriving = from_behind(output, "pp", 1)
            current = jnp.where(section_id == turn_index + 1, arriving, current)
    return result[None]


def inner_extent(mesh):
    row = mesh.devices[0]
    try:
        count = len({device.coords[1] for device in row})
    except AttributeError:
        count = 1
    return count if count > 1 and row.size % count == 0 else 1


def solution(mesh):
    pp_count, ep_count = mesh.devices.shape
    inner = inner_extent(mesh)
    split = Mesh(mesh.devices.reshape(pp_count, ep_count // inner, inner), ("pp", "ez", "ey"))
    ep = ("ez", "ey")
    placed = (
        P(ep, None),
        P("pp", None, None),
        P("pp", ep, None),
        P("pp", None),
        P("pp", ep, None, None),
        P("pp", ep, None, None),
    )
    return jax.shard_map(
        shards, mesh=split, in_specs=placed, out_specs=P("pp", ep, None), check_vma=False
    )
```

```python
import jax
import jax.numpy as jnp
from jax import lax
from jax.sharding import Mesh
from jax.sharding import PartitionSpec as P


def shards(tokens, routes, combine, norm_gain, expert_in, expert_out):
    outer = lax.axis_size("ez")
    inner = lax.axis_size("ey")
    group_size = outer * inner
    sections = lax.axis_size("pp")
    section_id = lax.axis_index("pp")
    member = lax.axis_index("ez") * inner + lax.axis_index("ey")
    tok_dev, model_width = tokens.shape
    top_count = routes.shape[2]
    capacity = tok_dev * top_count * 5 // (4 * group_size)
    hidden_units = expert_out.shape[2]
    slot_count = group_size * capacity
    section_routes = routes[0]
    experts_axis = jnp.arange(group_size, dtype=jnp.int32)
    start_row = member * tok_dev
    own_routes = lax.dynamic_slice_in_dim(section_routes, start_row, tok_dev, 0)
    flat_routes = own_routes.reshape(-1)
    one_hot = (flat_routes[:, None] == experts_axis[None, :]).astype(jnp.int32)
    earlier = jnp.cumsum(one_hot, axis=0) - one_hot
    rank_of = jnp.sum(earlier * one_hot, axis=1)
    slot_of = flat_routes * capacity + rank_of
    slot_grid = slot_of[None, :] == jnp.arange(slot_count, dtype=jnp.int32)[:, None]
    slot_grid = slot_grid.reshape(slot_count, tok_dev, top_count)
    picker = jnp.any(slot_grid, axis=2).astype(jnp.bfloat16).reshape(outer, inner, capacity, tok_dev)
    weigher = jnp.sum(jnp.where(slot_grid, combine[0][None, :, :], 0.0), axis=2).T
    weigher = weigher.reshape(tok_dev, outer, inner, capacity)
    first_weights = expert_in[0, 0]
    second_weights = expert_out[0, 0]
    gain_row = norm_gain[0]

    def layer(current):
        widened = current.astype(jnp.float32)
        scale = lax.rsqrt(jnp.mean(widened * widened, axis=-1, keepdims=True) + 1e-06)
        normed = (widened * scale * gain_row[None, :]).astype(jnp.bfloat16)
        packed = jnp.einsum("abct,td->abcd", picker, normed, preferred_element_type=jnp.float32)
        packed = packed.astype(jnp.bfloat16)
        stage = lax.all_to_all(packed, "ey", 1, 1, tiled=True)
        arrived = lax.all_to_all(stage, "ez", 0, 0, tiled=True)
        projected = jnp.einsum("abcd,dh->abch", arrived, first_weights, preferred_element_type=jnp.float32)
        hidden = (jax.nn.silu(projected[..., :hidden_units]) * projected[..., hidden_units:]).astype(
            jnp.bfloat16
        )
        produced = jnp.einsum("abch,hd->abcd", hidden, second_weights, preferred_element_type=jnp.float32)
        produced = produced.astype(jnp.bfloat16)
        stage = lax.all_to_all(produced, "ez", 0, 0, tiled=True)
        returned = lax.all_to_all(stage, "ey", 1, 1, tiled=True)
        blended = jnp.einsum(
            "tabc,abcd->td",
            weigher,
            returned.astype(jnp.float32),
            precision=lax.Precision.HIGHEST,
        )
        return (widened + blended).astype(jnp.bfloat16)

    current = tokens
    result = tokens
    for turn_index in range(sections):
        output = lax.cond(section_id == turn_index, layer, lambda held: held, current)
        result = jnp.where(section_id == turn_index, output, result)
        if turn_index + 1 < sections:
            arriving = lax.ppermute(output, "pp", [(turn_index, turn_index + 1)])
            current = jnp.where(section_id == turn_index + 1, arriving, current)
    return result[None]


def inner_extent(mesh):
    row = mesh.devices[0]
    try:
        count = len({device.coords[1] for device in row})
    except AttributeError:
        count = 1
    return count if count > 1 and row.size % count == 0 else 1


def solution(mesh):
    pp_count, ep_count = mesh.devices.shape
    inner = inner_extent(mesh)
    split = Mesh(mesh.devices.reshape(pp_count, ep_count // inner, inner), ("pp", "ez", "ey"))
    ep = ("ez", "ey")
    placed = (
        P(ep, None),
        P("pp", None, None),
        P("pp", ep, None),
        P("pp", None),
        P("pp", ep, None, None),
        P("pp", ep, None, None),
    )
    return jax.shard_map(
        shards, mesh=split, in_specs=placed, out_specs=P("pp", ep, None), check_vma=False
    )
```

```python
import jax
import jax.numpy as jnp
from jax import lax
from jax.sharding import PartitionSpec as P


def shards(tokens, routes, combine, norm_gain, expert_in, expert_out):
    group_size = lax.axis_size("ep")
    sections = lax.axis_size("pp")
    section_id = lax.axis_index("pp")
    member = lax.axis_index("ep")
    tok_dev, model_width = tokens.shape
    top_count = routes.shape[2]
    capacity = tok_dev * top_count * 5 // (4 * group_size)
    hidden_units = expert_out.shape[2]
    slot_count = group_size * capacity
    section_routes = routes[0]
    experts_axis = jnp.arange(group_size, dtype=jnp.int32)
    start_row = member * tok_dev
    own_routes = lax.dynamic_slice_in_dim(section_routes, start_row, tok_dev, 0)
    flat_routes = own_routes.reshape(-1)
    one_hot = (flat_routes[:, None] == experts_axis[None, :]).astype(jnp.int32)
    earlier = jnp.cumsum(one_hot, axis=0) - one_hot
    rank_of = jnp.sum(earlier * one_hot, axis=1)
    slot_of = flat_routes * capacity + rank_of
    slot_grid = slot_of[None, :] == jnp.arange(slot_count, dtype=jnp.int32)[:, None]
    slot_grid = slot_grid.reshape(slot_count, tok_dev, top_count)
    picker = jnp.any(slot_grid, axis=2).astype(jnp.bfloat16).reshape(group_size, capacity, tok_dev)
    weigher = jnp.sum(jnp.where(slot_grid, combine[0][None, :, :], 0.0), axis=2).T
    weigher = weigher.reshape(tok_dev, group_size, capacity)
    first_weights = expert_in[0, 0]
    second_weights = expert_out[0, 0]
    gain_row = norm_gain[0]

    def layer(current):
        widened = current.astype(jnp.float32)
        scale = lax.rsqrt(jnp.mean(widened * widened, axis=-1, keepdims=True) + 1e-06)
        normed = (widened * scale * gain_row[None, :]).astype(jnp.bfloat16)
        packed = jnp.einsum("gct,td->gcd", picker, normed, preferred_element_type=jnp.float32)
        arrived = lax.all_to_all(packed.astype(jnp.bfloat16), "ep", 0, 0, tiled=True)
        projected = jnp.einsum("gcd,dh->gch", arrived, first_weights, preferred_element_type=jnp.float32)
        hidden = (jax.nn.silu(projected[..., :hidden_units]) * projected[..., hidden_units:]).astype(
            jnp.bfloat16
        )
        produced = jnp.einsum("gch,hd->gcd", hidden, second_weights, preferred_element_type=jnp.float32)
        returned = lax.all_to_all(produced.astype(jnp.bfloat16), "ep", 0, 0, tiled=True)
        blended = jnp.einsum(
            "tgc,gcd->td",
            weigher,
            returned.astype(jnp.float32),
            precision=lax.Precision.HIGHEST,
        )
        return (widened + blended).astype(jnp.bfloat16)

    current = tokens
    result = tokens
    for turn_index in range(sections):
        output = lax.cond(section_id == turn_index, layer, lambda held: held, current)
        result = jnp.where(section_id == turn_index, output, result)
        if turn_index + 1 < sections:
            arriving = lax.ppermute(output, "pp", [(turn_index, turn_index + 1)])
            current = jnp.where(section_id == turn_index + 1, arriving, current)
    return result[None]


def solution(mesh):
    placed = (
        P("ep", None),
        P("pp", None, None),
        P("pp", "ep", None),
        P("pp", None),
        P("pp", "ep", None, None),
        P("pp", "ep", None, None),
    )
    return jax.shard_map(
        shards, mesh=mesh, in_specs=placed, out_specs=P("pp", "ep", None), check_vma=False
    )
```

```python
import jax
import jax.numpy as jnp
from jax import lax
from jax.sharding import PartitionSpec as P


def shards(tokens, routes, combine, norm_gain, expert_in, expert_out):
    group_size = lax.axis_size("ep")
    sections = lax.axis_size("pp")
    section_id = lax.axis_index("pp")
    member = lax.axis_index("ep")
    tok_dev, model_width = tokens.shape
    top_count = routes.shape[2]
    capacity = tok_dev * top_count * 5 // (4 * group_size)
    hidden_units = expert_out.shape[2]
    slot_count = group_size * capacity
    section_routes = routes[0]
    experts_axis = jnp.arange(group_size, dtype=jnp.int32)
    start_row = member * tok_dev
    own_routes = lax.dynamic_slice_in_dim(section_routes, start_row, tok_dev, 0)
    flat_routes = own_routes.reshape(-1)
    one_hot = (flat_routes[:, None] == experts_axis[None, :]).astype(jnp.int32)
    earlier = jnp.cumsum(one_hot, axis=0) - one_hot
    rank_of = jnp.sum(earlier * one_hot, axis=1)
    slot_of = flat_routes * capacity + rank_of
    slot_grid = slot_of[None, :] == jnp.arange(slot_count, dtype=jnp.int32)[:, None]
    slot_grid = slot_grid.reshape(slot_count, tok_dev, top_count)
    picker = jnp.any(slot_grid, axis=2).astype(jnp.bfloat16).reshape(group_size, capacity, tok_dev)
    weigher = jnp.sum(jnp.where(slot_grid, combine[0][None, :, :], 0.0), axis=2).T
    weigher = weigher.reshape(tok_dev, group_size, capacity)
    first_weights = expert_in[0, 0]
    second_weights = expert_out[0, 0]
    gain_row = norm_gain[0]

    def exchange(blocks):
        lanes = 128 if model_width % 128 == 0 else model_width
        dense = blocks.reshape(group_size, capacity * (model_width // lanes), lanes)
        moved = lax.all_to_all(dense, "ep", 0, 0, tiled=True)
        return moved.reshape(blocks.shape)

    def layer(current):
        widened = current.astype(jnp.float32)
        scale = lax.rsqrt(jnp.mean(widened * widened, axis=-1, keepdims=True) + 1e-06)
        normed = (widened * scale * gain_row[None, :]).astype(jnp.bfloat16)
        packed = jnp.einsum("gct,td->gcd", picker, normed, preferred_element_type=jnp.float32)
        arrived = exchange(packed.astype(jnp.bfloat16))
        projected = jnp.einsum("gcd,dh->gch", arrived, first_weights, preferred_element_type=jnp.float32)
        hidden = (jax.nn.silu(projected[..., :hidden_units]) * projected[..., hidden_units:]).astype(
            jnp.bfloat16
        )
        produced = jnp.einsum("gch,hd->gcd", hidden, second_weights, preferred_element_type=jnp.float32)
        returned = exchange(produced.astype(jnp.bfloat16))
        blended = jnp.einsum(
            "tgc,gcd->td",
            weigher,
            returned.astype(jnp.float32),
            precision=lax.Precision.HIGHEST,
        )
        return (widened + blended).astype(jnp.bfloat16)

    current = tokens
    result = tokens
    for turn_index in range(sections):
        output = lax.cond(section_id == turn_index, layer, lambda held: held, current)
        result = jnp.where(section_id == turn_index, output, result)
        if turn_index + 1 < sections:
            arriving = lax.ppermute(output, "pp", [(turn_index, turn_index + 1)])
            current = jnp.where(section_id == turn_index + 1, arriving, current)
    return result[None]


def solution(mesh):
    placed = (
        P("ep", None),
        P("pp", None, None),
        P("pp", "ep", None),
        P("pp", None),
        P("pp", "ep", None, None),
        P("pp", "ep", None, None),
    )
    return jax.shard_map(
        shards, mesh=mesh, in_specs=placed, out_specs=P("pp", "ep", None), check_vma=False
    )
```

```python
import jax
import jax.numpy as jnp
from jax import lax
from jax.sharding import PartitionSpec as P


def shards(tokens, routes, combine, norm_gain, expert_in, expert_out):
    group_size = lax.axis_size("ep")
    sections = lax.axis_size("pp")
    section_id = lax.axis_index("pp")
    member = lax.axis_index("ep")
    tok_dev, model_width = tokens.shape
    top_count = routes.shape[2]
    capacity = tok_dev * top_count * 5 // (4 * group_size)
    hidden_units = expert_out.shape[2]
    slot_count = group_size * capacity
    section_routes = routes[0]
    experts_axis = jnp.arange(group_size, dtype=jnp.int32)
    start_row = member * tok_dev
    own_routes = lax.dynamic_slice_in_dim(section_routes, start_row, tok_dev, 0)
    flat_routes = own_routes.reshape(-1)
    one_hot = (flat_routes[:, None] == experts_axis[None, :]).astype(jnp.int32)
    earlier = jnp.cumsum(one_hot, axis=0) - one_hot
    rank_of = jnp.sum(earlier * one_hot, axis=1)
    slot_of = flat_routes * capacity + rank_of
    slot_grid = slot_of[None, :] == jnp.arange(slot_count, dtype=jnp.int32)[:, None]
    slot_grid = slot_grid.reshape(slot_count, tok_dev, top_count)
    picker = jnp.any(slot_grid, axis=2).astype(jnp.bfloat16).reshape(group_size, capacity, tok_dev)
    weigher = jnp.sum(jnp.where(slot_grid, combine[0][None, :, :], 0.0), axis=2).T
    weigher = weigher.reshape(tok_dev, group_size, capacity)
    first_weights = expert_in[0, 0]
    second_weights = expert_out[0, 0]
    gain_row = norm_gain[0]

    lanes = 128 if model_width % 128 == 0 else model_width
    rows = model_width // lanes

    def exchange(blocks):
        dense = blocks.reshape(group_size, capacity * rows, lanes)
        moved = lax.all_to_all(dense, "ep", 0, 0, tiled=True)
        return moved.reshape(blocks.shape)

    def layer(current):
        widened = current.astype(jnp.float32)
        scale = lax.rsqrt(jnp.mean(widened * widened, axis=-1, keepdims=True) + 1e-06)
        normed = (widened * scale * gain_row[None, :]).astype(jnp.bfloat16)
        packed = jnp.einsum(
            "gct,tjk->gcjk", picker, normed.reshape(tok_dev, rows, lanes), preferred_element_type=jnp.float32
        )
        arrived = exchange(packed.astype(jnp.bfloat16))
        projected = jnp.einsum(
            "gcjk,jkh->gch", arrived, first_weights.reshape(rows, lanes, -1), preferred_element_type=jnp.float32
        )
        hidden = (jax.nn.silu(projected[..., :hidden_units]) * projected[..., hidden_units:]).astype(
            jnp.bfloat16
        )
        produced = jnp.einsum("gch,hd->gcd", hidden, second_weights, preferred_element_type=jnp.float32)
        returned = exchange(produced.astype(jnp.bfloat16))
        blended = jnp.einsum(
            "tgc,gcd->td",
            weigher,
            returned.astype(jnp.float32),
            precision=lax.Precision.HIGHEST,
        )
        return (widened + blended).astype(jnp.bfloat16)

    def step(held):
        output = layer(held[0])
        return output, output

    current = tokens
    result = tokens
    for turn_index in range(sections):
        output, result = lax.cond(section_id == turn_index, step, lambda held: held, (current, result))
        if turn_index + 1 < sections:
            current = lax.ppermute(output, "pp", [(turn_index, turn_index + 1)])
    return result[None]


def solution(mesh):
    placed = (
        P("ep", None),
        P("pp", None, None),
        P("pp", "ep", None),
        P("pp", None),
        P("pp", "ep", None, None),
        P("pp", "ep", None, None),
    )
    return jax.shard_map(
        shards, mesh=mesh, in_specs=placed, out_specs=P("pp", "ep", None), check_vma=False
    )
```

```python
import jax
import jax.numpy as jnp
from jax import lax
from jax.sharding import PartitionSpec as P


def shards(tokens, routes, combine, norm_gain, expert_in, expert_out):
    group_size = lax.axis_size("ep")
    sections = lax.axis_size("pp")
    section_id = lax.axis_index("pp")
    member = lax.axis_index("ep")
    tok_dev, model_width = tokens.shape
    top_count = routes.shape[2]
    capacity = tok_dev * top_count * 5 // (4 * group_size)
    hidden_units = expert_out.shape[2]
    slot_count = group_size * capacity
    section_routes = routes[0]
    experts_axis = jnp.arange(group_size, dtype=jnp.int32)
    start_row = member * tok_dev
    own_routes = lax.dynamic_slice_in_dim(section_routes, start_row, tok_dev, 0)
    flat_routes = own_routes.reshape(-1)
    one_hot = (flat_routes[:, None] == experts_axis[None, :]).astype(jnp.int32)
    earlier = jnp.cumsum(one_hot, axis=0) - one_hot
    rank_of = jnp.sum(earlier * one_hot, axis=1)
    slot_of = flat_routes * capacity + rank_of
    slot_grid = slot_of[None, :] == jnp.arange(slot_count, dtype=jnp.int32)[:, None]
    slot_grid = slot_grid.reshape(slot_count, tok_dev, top_count)
    picker = jnp.any(slot_grid, axis=2).astype(jnp.bfloat16).reshape(group_size, capacity, tok_dev)
    weigher = jnp.sum(jnp.where(slot_grid, combine[0][None, :, :], 0.0), axis=2).T
    weigher = weigher.reshape(tok_dev, group_size, capacity)
    first_weights = expert_in[0, 0]
    second_weights = expert_out[0, 0]
    gain_row = norm_gain[0]

    lanes = 128 if model_width % 128 == 0 else model_width
    rows = model_width // lanes

    def exchange(blocks):
        dense = blocks.reshape(group_size, capacity * rows, lanes)
        moved = lax.all_to_all(dense, "ep", 0, 0, tiled=True)
        return moved.reshape(blocks.shape)

    def layer(current):
        widened = current.astype(jnp.float32)
        scale = lax.rsqrt(jnp.mean(widened * widened, axis=-1, keepdims=True) + 1e-06)
        normed = (widened * scale * gain_row[None, :]).astype(jnp.bfloat16)
        packed = jnp.einsum(
            "gct,tjk->gcjk", picker, normed.reshape(tok_dev, rows, lanes), preferred_element_type=jnp.float32
        )
        arrived = exchange(packed.astype(jnp.bfloat16))
        projected = jnp.einsum(
            "gcjk,jkh->gch", arrived, first_weights.reshape(rows, lanes, -1), preferred_element_type=jnp.float32
        )
        hidden = (jax.nn.silu(projected[..., :hidden_units]) * projected[..., hidden_units:]).astype(
            jnp.bfloat16
        )
        produced = jnp.einsum("gch,hd->gcd", hidden, second_weights, preferred_element_type=jnp.float32)
        returned = lax.all_to_all(
            produced.astype(jnp.bfloat16).reshape(group_size, capacity * rows, lanes), "ep", 0, 0, tiled=True
        )
        blended = jnp.einsum(
            "tgc,gcjk->tjk",
            weigher,
            returned.reshape(group_size, capacity, rows, lanes).astype(jnp.float32),
            precision=lax.Precision.HIGHEST,
        ).reshape(tok_dev, model_width)
        return (widened + blended).astype(jnp.bfloat16)

    def step(held):
        output = layer(held[0])
        return output, output

    current = tokens
    result = tokens
    for turn_index in range(sections):
        output, result = lax.cond(section_id == turn_index, step, lambda held: held, (current, result))
        if turn_index + 1 < sections:
            current = lax.ppermute(output, "pp", [(turn_index, turn_index + 1)])
    return result[None]


def solution(mesh):
    placed = (
        P("ep", None),
        P("pp", None, None),
        P("pp", "ep", None),
        P("pp", None),
        P("pp", "ep", None, None),
        P("pp", "ep", None, None),
    )
    return jax.shard_map(
        shards, mesh=mesh, in_specs=placed, out_specs=P("pp", "ep", None), check_vma=False
    )
```

```python
import jax
import jax.numpy as jnp
from jax import lax
from jax.sharding import PartitionSpec as P


def shards(tokens, routes, combine, norm_gain, expert_in, expert_out):
    group_size = lax.axis_size("ep")
    sections = lax.axis_size("pp")
    section_id = lax.axis_index("pp")
    member = lax.axis_index("ep")
    tok_dev, model_width = tokens.shape
    top_count = routes.shape[2]
    capacity = tok_dev * top_count * 5 // (4 * group_size)
    hidden_units = expert_out.shape[2]
    slot_count = group_size * capacity
    section_routes = routes[0]
    experts_axis = jnp.arange(group_size, dtype=jnp.int32)
    start_row = member * tok_dev
    own_routes = lax.dynamic_slice_in_dim(section_routes, start_row, tok_dev, 0)
    flat_routes = own_routes.reshape(-1)
    one_hot = (flat_routes[:, None] == experts_axis[None, :]).astype(jnp.int32)
    earlier = jnp.cumsum(one_hot, axis=0) - one_hot
    rank_of = jnp.sum(earlier * one_hot, axis=1)
    slot_of = flat_routes * capacity + rank_of
    slot_grid = slot_of[None, :] == jnp.arange(slot_count, dtype=jnp.int32)[:, None]
    slot_grid = slot_grid.reshape(slot_count, tok_dev, top_count)
    picker = jnp.any(slot_grid, axis=2).astype(jnp.bfloat16).reshape(group_size, capacity, tok_dev)
    weigher = jnp.sum(jnp.where(slot_grid, combine[0][None, :, :], 0.0), axis=2).T
    weigher = weigher.reshape(tok_dev, group_size, capacity)
    first_weights = expert_in[0, 0]
    second_weights = expert_out[0, 0]
    gain_row = norm_gain[0]

    lanes = 128 if model_width % 128 == 0 else model_width
    rows = model_width // lanes

    tiled_second = lax.optimization_barrier(second_weights.reshape(hidden_units, rows, lanes))

    def exchange(blocks):
        dense = blocks.reshape(group_size, capacity * rows, lanes)
        moved = lax.all_to_all(dense, "ep", 0, 0, tiled=True)
        return moved.reshape(blocks.shape)

    def layer(current):
        widened = current.astype(jnp.float32)
        scale = lax.rsqrt(jnp.mean(widened * widened, axis=-1, keepdims=True) + 1e-06)
        normed = (widened * scale * gain_row[None, :]).astype(jnp.bfloat16)
        packed = jnp.einsum(
            "gct,tjk->gcjk", picker, normed.reshape(tok_dev, rows, lanes), preferred_element_type=jnp.float32
        )
        arrived = exchange(packed.astype(jnp.bfloat16))
        projected = jnp.einsum(
            "gcjk,jkh->gch", arrived, first_weights.reshape(rows, lanes, -1), preferred_element_type=jnp.float32
        )
        hidden = (jax.nn.silu(projected[..., :hidden_units]) * projected[..., hidden_units:]).astype(
            jnp.bfloat16
        )
        produced = jnp.einsum("gch,hjk->gcjk", hidden, tiled_second, preferred_element_type=jnp.float32)
        returned = lax.all_to_all(
            produced.astype(jnp.bfloat16).reshape(group_size, capacity * rows, lanes), "ep", 0, 0, tiled=True
        )
        blended = jnp.einsum(
            "tgc,gcjk->tjk",
            weigher,
            returned.reshape(group_size, capacity, rows, lanes).astype(jnp.float32),
            precision=lax.Precision.HIGHEST,
        ).reshape(tok_dev, model_width)
        return (widened + blended).astype(jnp.bfloat16)

    def step(held):
        output = layer(held[0])
        return output, output

    current = tokens
    result = tokens
    for turn_index in range(sections):
        output, result = lax.cond(section_id == turn_index, step, lambda held: held, (current, result))
        if turn_index + 1 < sections:
            current = lax.ppermute(output, "pp", [(turn_index, turn_index + 1)])
    return result[None]


def solution(mesh):
    placed = (
        P("ep", None),
        P("pp", None, None),
        P("pp", "ep", None),
        P("pp", None),
        P("pp", "ep", None, None),
        P("pp", "ep", None, None),
    )
    return jax.shard_map(
        shards, mesh=mesh, in_specs=placed, out_specs=P("pp", "ep", None), check_vma=False
    )
```

```python
import jax
import jax.numpy as jnp
from jax import lax
from jax.sharding import PartitionSpec as P


def shards(tokens, routes, combine, norm_gain, expert_in, expert_out):
    group_size = lax.axis_size("ep")
    sections = lax.axis_size("pp")
    section_id = lax.axis_index("pp")
    member = lax.axis_index("ep")
    tok_dev, model_width = tokens.shape
    top_count = routes.shape[2]
    capacity = tok_dev * top_count * 5 // (4 * group_size)
    hidden_units = expert_out.shape[2]
    slot_count = group_size * capacity
    section_routes = routes[0]
    experts_axis = jnp.arange(group_size, dtype=jnp.int32)
    start_row = member * tok_dev
    own_routes = lax.dynamic_slice_in_dim(section_routes, start_row, tok_dev, 0)
    flat_routes = own_routes.reshape(-1)
    one_hot = (flat_routes[:, None] == experts_axis[None, :]).astype(jnp.int32)
    earlier = jnp.cumsum(one_hot, axis=0) - one_hot
    rank_of = jnp.sum(earlier * one_hot, axis=1)
    slot_of = flat_routes * capacity + rank_of
    slot_grid = slot_of[None, :] == jnp.arange(slot_count, dtype=jnp.int32)[:, None]
    slot_grid = slot_grid.reshape(slot_count, tok_dev, top_count)
    picker = jnp.any(slot_grid, axis=2).astype(jnp.bfloat16).reshape(group_size, capacity, tok_dev)
    weigher = jnp.sum(jnp.where(slot_grid, combine[0][None, :, :], 0.0), axis=2).T
    weigher = weigher.reshape(tok_dev, group_size, capacity)
    first_weights = expert_in[0, 0]
    second_weights = expert_out[0, 0]
    gain_row = norm_gain[0]

    lanes = 128 if model_width % 128 == 0 else model_width
    rows = model_width // lanes

    tiled_second = lax.optimization_barrier(second_weights.reshape(hidden_units, rows, lanes))

    def exchange(blocks):
        dense = blocks.reshape(group_size, capacity * rows, lanes)
        moved = lax.all_to_all(dense, "ep", 0, 0, tiled=True)
        return moved.reshape(blocks.shape)

    def layer(current):
        widened = current.astype(jnp.float32)
        scale = lax.rsqrt(jnp.mean(widened * widened, axis=-1, keepdims=True) + 1e-06)
        normed = (widened * scale * gain_row[None, :]).astype(jnp.bfloat16)
        packed = jnp.einsum(
            "gct,tjk->gcjk", picker, normed.reshape(tok_dev, rows, lanes), preferred_element_type=jnp.float32
        )
        arrived = exchange(packed.astype(jnp.bfloat16))
        projected = jnp.einsum(
            "gcjk,jkh->gch", arrived, first_weights.reshape(rows, lanes, -1), preferred_element_type=jnp.float32
        )
        hidden = (jax.nn.silu(projected[..., :hidden_units]) * projected[..., hidden_units:]).astype(
            jnp.bfloat16
        )
        produced = jnp.einsum("gch,hjk->gcjk", hidden, tiled_second, preferred_element_type=jnp.float32)
        returned = lax.all_to_all(
            produced.astype(jnp.bfloat16).reshape(group_size, capacity * rows, lanes), "ep", 0, 0, tiled=True
        )
        blended = jnp.einsum(
            "tgc,gcjk->tjk",
            weigher,
            returned.reshape(group_size, capacity, rows, lanes).astype(jnp.float32),
            precision=lax.Precision.HIGHEST,
        ).reshape(tok_dev, model_width)
        return (widened + blended).astype(jnp.bfloat16)

    def step(held):
        output = layer(held[0])
        return output, output

    ring = [(i, i + 1) for i in range(sections - 1)]

    def turn(turn_index, held):
        output, result = lax.cond(section_id == turn_index, step, lambda kept: kept, held)
        return lax.ppermute(output, "pp", ring), result

    _, result = lax.fori_loop(0, sections, turn, (tokens, tokens))
    return result[None]


def solution(mesh):
    placed = (
        P("ep", None),
        P("pp", None, None),
        P("pp", "ep", None),
        P("pp", None),
        P("pp", "ep", None, None),
        P("pp", "ep", None, None),
    )
    return jax.shard_map(
        shards, mesh=mesh, in_specs=placed, out_specs=P("pp", "ep", None), check_vma=False
    )
```

```python
import jax
import jax.numpy as jnp
from jax import lax
from jax.sharding import PartitionSpec as P


def shards(tokens, routes, combine, norm_gain, expert_in, expert_out):
    group_size = lax.axis_size("ep")
    sections = lax.axis_size("pp")
    section_id = lax.axis_index("pp")
    member = lax.axis_index("ep")
    tok_dev, model_width = tokens.shape
    top_count = routes.shape[2]
    capacity = tok_dev * top_count * 5 // (4 * group_size)
    hidden_units = expert_out.shape[2]
    slot_count = group_size * capacity
    section_routes = routes[0]
    experts_axis = jnp.arange(group_size, dtype=jnp.int32)
    start_row = member * tok_dev
    own_routes = lax.dynamic_slice_in_dim(section_routes, start_row, tok_dev, 0)
    flat_routes = own_routes.reshape(-1)
    one_hot = (flat_routes[:, None] == experts_axis[None, :]).astype(jnp.int32)
    earlier = jnp.cumsum(one_hot, axis=0) - one_hot
    rank_of = jnp.sum(earlier * one_hot, axis=1)
    slot_of = flat_routes * capacity + rank_of
    slot_grid = slot_of[None, :] == jnp.arange(slot_count, dtype=jnp.int32)[:, None]
    slot_grid = slot_grid.reshape(slot_count, tok_dev, top_count)
    picker = jnp.any(slot_grid, axis=2).astype(jnp.bfloat16).reshape(group_size, capacity, tok_dev)
    weigher = jnp.sum(jnp.where(slot_grid, combine[0][None, :, :], 0.0), axis=2).T
    weigher = weigher.reshape(tok_dev, group_size, capacity)
    first_weights = expert_in[0, 0]
    second_weights = expert_out[0, 0]
    gain_row = norm_gain[0]

    lanes = 128 if model_width % 128 == 0 else model_width
    rows = model_width // lanes

    def exchange(blocks):
        dense = blocks.reshape(group_size, capacity * rows, lanes)
        moved = lax.all_to_all(dense, "ep", 0, 0, tiled=True)
        return moved.reshape(blocks.shape)

    def layer(current, down_weights):
        widened = current.astype(jnp.float32)
        scale = lax.rsqrt(jnp.mean(widened * widened, axis=-1, keepdims=True) + 1e-06)
        normed = (widened * scale * gain_row[None, :]).astype(jnp.bfloat16)
        packed = jnp.einsum(
            "gct,tjk->gcjk", picker, normed.reshape(tok_dev, rows, lanes), preferred_element_type=jnp.float32
        )
        arrived = exchange(packed.astype(jnp.bfloat16))
        projected = jnp.einsum(
            "gcjk,jkh->gch", arrived, first_weights.reshape(rows, lanes, -1), preferred_element_type=jnp.float32
        )
        hidden = (jax.nn.silu(projected[..., :hidden_units]) * projected[..., hidden_units:]).astype(
            jnp.bfloat16
        )
        produced = jnp.einsum("gch,hjk->gcjk", hidden, down_weights, preferred_element_type=jnp.float32)
        returned = lax.all_to_all(
            produced.astype(jnp.bfloat16).reshape(group_size, capacity * rows, lanes), "ep", 0, 0, tiled=True
        )
        blended = jnp.einsum(
            "tgc,gcjk->tjk",
            weigher,
            returned.reshape(group_size, capacity, rows, lanes).astype(jnp.float32),
            precision=lax.Precision.HIGHEST,
        ).reshape(tok_dev, model_width)
        return (widened + blended).astype(jnp.bfloat16)

    ring = [(i, i + 1) for i in range(sections - 1)]
    plain_second = second_weights.reshape(hidden_units, rows, lanes)

    def first_step(held):
        output = layer(held[0], plain_second)
        return output, output

    output, result = lax.cond(section_id == 0, first_step, lambda kept: kept, (tokens, tokens))
    current = lax.ppermute(output, "pp", ring)
    tiled_second, current = lax.optimization_barrier((plain_second, current))

    def step(held):
        output = layer(held[0], tiled_second)
        return output, output

    def turn(turn_index, held):
        output, result = lax.cond(section_id == turn_index, step, lambda kept: kept, held)
        return lax.ppermute(output, "pp", ring), result

    _, result = lax.fori_loop(1, sections, turn, (current, result))
    return result[None]


def solution(mesh):
    placed = (
        P("ep", None),
        P("pp", None, None),
        P("pp", "ep", None),
        P("pp", None),
        P("pp", "ep", None, None),
        P("pp", "ep", None, None),
    )
    return jax.shard_map(
        shards, mesh=mesh, in_specs=placed, out_specs=P("pp", "ep", None), check_vma=False
    )
```

```python
import jax
import jax.numpy as jnp
from jax import lax
from jax.sharding import PartitionSpec as P


def shards(tokens, routes, combine, norm_gain, expert_in, expert_out):
    group_size = lax.axis_size("ep")
    sections = lax.axis_size("pp")
    section_id = lax.axis_index("pp")
    member = lax.axis_index("ep")
    tok_dev, model_width = tokens.shape
    top_count = routes.shape[2]
    capacity = tok_dev * top_count * 5 // (4 * group_size)
    hidden_units = expert_out.shape[2]
    slot_count = group_size * capacity
    section_routes = routes[0]
    experts_axis = jnp.arange(group_size, dtype=jnp.int32)
    start_row = member * tok_dev
    own_routes = lax.dynamic_slice_in_dim(section_routes, start_row, tok_dev, 0)
    flat_routes = own_routes.reshape(-1)
    one_hot = (flat_routes[:, None] == experts_axis[None, :]).astype(jnp.int32)
    earlier = jnp.cumsum(one_hot, axis=0) - one_hot
    rank_of = jnp.sum(earlier * one_hot, axis=1)
    slot_of = flat_routes * capacity + rank_of
    slot_grid = slot_of[None, :] == jnp.arange(slot_count, dtype=jnp.int32)[:, None]
    slot_grid = slot_grid.reshape(slot_count, tok_dev, top_count)
    picker = jnp.any(slot_grid, axis=2).astype(jnp.bfloat16).reshape(group_size, capacity, tok_dev)
    weigher = jnp.sum(jnp.where(slot_grid, combine[0][None, :, :], 0.0), axis=2).T
    weigher = weigher.reshape(tok_dev, group_size, capacity)
    first_weights = expert_in[0, 0]
    second_weights = expert_out[0, 0]
    gain_row = norm_gain[0]

    lanes = 128 if model_width % 128 == 0 else model_width
    rows = model_width // lanes

    tiled_second = lax.optimization_barrier(second_weights.reshape(hidden_units, rows, lanes))

    def exchange(blocks):
        dense = blocks.reshape(group_size, capacity * rows, lanes)
        moved = lax.all_to_all(dense, "ep", 0, 0, tiled=True)
        return moved.reshape(blocks.shape)

    def layer(current):
        widened = current.astype(jnp.float32)
        scale = lax.rsqrt(jnp.mean(widened * widened, axis=-1, keepdims=True) + 1e-06)
        normed = (widened * scale * gain_row[None, :]).astype(jnp.bfloat16)
        packed = jnp.einsum(
            "gct,tjk->gcjk", picker, normed.reshape(tok_dev, rows, lanes), preferred_element_type=jnp.float32
        )
        arrived = exchange(packed.astype(jnp.bfloat16))
        projected = jnp.einsum(
            "gcjk,jkh->gch", arrived, first_weights.reshape(rows, lanes, -1), preferred_element_type=jnp.float32
        )
        hidden = (jax.nn.silu(projected[..., :hidden_units]) * projected[..., hidden_units:]).astype(
            jnp.bfloat16
        )
        produced = jnp.einsum("gch,hjk->gcjk", hidden, tiled_second, preferred_element_type=jnp.float32)
        returned = lax.all_to_all(
            produced.astype(jnp.bfloat16).reshape(group_size, capacity * rows, lanes), "ep", 0, 0, tiled=True
        )
        blended = jnp.einsum(
            "tgc,gcjk->tjk",
            weigher,
            returned.reshape(group_size, capacity, rows, lanes).astype(jnp.float32),
            precision=lax.Precision.HIGHEST,
        ).reshape(tok_dev, model_width)
        return (widened + blended).astype(jnp.bfloat16)

    def step(held):
        output = layer(held[0])
        return output, output

    ring = [(i, i + 1) for i in range(sections - 1)]

    def turn(turn_index, held):
        output, result = lax.cond(section_id == turn_index, step, lambda kept: kept, held)
        return lax.ppermute(output, "pp", ring), result

    held = lax.fori_loop(0, sections - 1, turn, (tokens, tokens))
    _, result = lax.cond(section_id == sections - 1, step, lambda kept: kept, held)
    return result[None]


def solution(mesh):
    placed = (
        P("ep", None),
        P("pp", None, None),
        P("pp", "ep", None),
        P("pp", None),
        P("pp", "ep", None, None),
        P("pp", "ep", None, None),
    )
    return jax.shard_map(
        shards, mesh=mesh, in_specs=placed, out_specs=P("pp", "ep", None), check_vma=False
    )
```

```python
import jax
import jax.numpy as jnp
from jax import lax
from jax.sharding import PartitionSpec as P


def shards(tokens, routes, combine, norm_gain, expert_in, expert_out):
    group_size = lax.axis_size("ep")
    sections = lax.axis_size("pp")
    section_id = lax.axis_index("pp")
    member = lax.axis_index("ep")
    tok_dev, model_width = tokens.shape
    top_count = routes.shape[2]
    capacity = tok_dev * top_count * 5 // (4 * group_size)
    hidden_units = expert_out.shape[2]
    slot_count = group_size * capacity
    section_routes = routes[0]
    experts_axis = jnp.arange(group_size, dtype=jnp.int32)
    start_row = member * tok_dev
    own_routes = lax.dynamic_slice_in_dim(section_routes, start_row, tok_dev, 0)
    flat_routes = own_routes.reshape(-1)
    one_hot = (flat_routes[:, None] == experts_axis[None, :]).astype(jnp.int32)
    earlier = jnp.cumsum(one_hot, axis=0) - one_hot
    rank_of = jnp.sum(earlier * one_hot, axis=1)
    slot_of = flat_routes * capacity + rank_of
    slot_grid = slot_of[None, :] == jnp.arange(slot_count, dtype=jnp.int32)[:, None]
    slot_grid = slot_grid.reshape(slot_count, tok_dev, top_count)
    picker = jnp.any(slot_grid, axis=2).astype(jnp.bfloat16).reshape(group_size, capacity, tok_dev)
    weigher = jnp.sum(jnp.where(slot_grid, combine[0][None, :, :], 0.0), axis=2).T
    weigher = weigher.reshape(tok_dev, group_size, capacity)
    first_weights = expert_in[0, 0]
    second_weights = expert_out[0, 0]
    gain_row = norm_gain[0]

    lanes = 128 if model_width % 128 == 0 else model_width
    rows = model_width // lanes

    tiled_second = lax.optimization_barrier(second_weights.reshape(hidden_units, rows, lanes))

    def exchange(blocks):
        dense = blocks.reshape(group_size, capacity * rows, lanes)
        moved = lax.all_to_all(dense, "ep", 0, 0, tiled=True)
        return moved.reshape(blocks.shape)

    def layer(current):
        widened = current.astype(jnp.float32)
        scale = lax.rsqrt(jnp.mean(widened * widened, axis=-1, keepdims=True) + 1e-06)
        normed = (widened * scale * gain_row[None, :]).astype(jnp.bfloat16)
        packed = jnp.einsum(
            "gct,tjk->gcjk", picker, normed.reshape(tok_dev, rows, lanes), preferred_element_type=jnp.float32
        )
        arrived = exchange(packed.astype(jnp.bfloat16))
        projected = jnp.einsum(
            "gcjk,jkh->gch", arrived, first_weights.reshape(rows, lanes, -1), preferred_element_type=jnp.float32
        )
        hidden = (jax.nn.silu(projected[..., :hidden_units]) * projected[..., hidden_units:]).astype(
            jnp.bfloat16
        )
        produced = jnp.einsum("gch,hjk->gcjk", hidden, tiled_second, preferred_element_type=jnp.float32)
        returned = lax.all_to_all(
            produced.astype(jnp.bfloat16).reshape(group_size, capacity * rows, lanes), "ep", 0, 0, tiled=True
        )
        blended = jnp.einsum(
            "tgc,gcjk->tjk",
            weigher,
            returned.reshape(group_size, capacity, rows, lanes).astype(jnp.float32),
            precision=lax.Precision.HIGHEST,
        ).reshape(tok_dev, model_width)
        return (widened + blended).astype(jnp.bfloat16)

    def step(held):
        output = layer(held[0])
        return output, output

    ring = [(i, i + 1) for i in range(sections - 1)]

    def turn(turn_index, held):
        output, result = lax.cond(section_id == turn_index, step, lambda kept: kept, held)
        return lax.ppermute(output, "pp", ring), result

    _, result = lax.fori_loop(0, sections, turn, (tokens, tokens), unroll=2)
    return result[None]


def solution(mesh):
    placed = (
        P("ep", None),
        P("pp", None, None),
        P("pp", "ep", None),
        P("pp", None),
        P("pp", "ep", None, None),
        P("pp", "ep", None, None),
    )
    return jax.shard_map(
        shards, mesh=mesh, in_specs=placed, out_specs=P("pp", "ep", None), check_vma=False
    )
```
